256 devices in a mesh: space: 32 (over x, z), dp: 8 (over y, core).
Axes of the slice: x: 4, y: 4, z: 8, core: 2. Of those that a mesh axis runs over, the one named last changes fastest.
Arguments:
- features: bfloat16 [8, 16384, 128], P('dp', 'space'), may hold values from -6 to 6
- cotangent: bfloat16 [8, 16384, 128], P('dp', 'space'), may hold values from -6 to 6
- weight_one: bfloat16 [27, 128, 128], replicated, may hold values from -0.21875 to 0.21875
- weight_two: bfloat16 [27, 128, 128], replicated, may hold values from -0.21875 to 0.21875
- rules: int32 [8, 32, 2, 27, 256], P('dp', 'space'), may hold values from 0 to 1024, as said below
- halo_send: int32 [8, 32, 2, 2], P('dp', 'space'), may hold values from 0 to 3
- block_counts: int32 [8, 128], P('dp', 'space'), may hold values from 16 to 128
Outputs:
- grad_features: float32 [8, 16384, 128], P('dp', 'space')
- grad_one: float32 [27, 128, 128], replicated
- grad_two: float32 [27, 128, 128], replicated
The draws below stay inside these ranges and needn't reach their ends.
Inputs may be any that keep to these rules, and one draw needn't show every extreme that they name: `rules`: for each scene, slab and offset, the live slots come first and hold distinct targets and distinct sources; padding slots hold source 1024 and target 512; at least half of the slots are live, and offset 13 is full with each source equal to its target.
All inputs are finite; a program needn't handle non-finite values.
Results may differ from the reference program's by a relative error of at most 0.0032.
Values may be sent and summed in bfloat16 or wider, within the bound.
No kernel may reach another device: no remote copies, remote signals or barrier semaphores. Data moves between devices by JAX's collectives and lax.ppermute only.
A program may use at most 64 MiB of HBM per device.

```python
import jax
import jax.numpy as jnp
from jax import lax

C = 128
K = 27
BLOCK = 128
BLK_DEV = 4
HB = 2
SCENES = 8
SLABS = 32
ROWS_DEV = 512
NROWS = 16384
NBLOCKS = 128
RULES = 256
HALO = 256
EXT = 1024


def draw_rules(key, part):
    total = SCENES * SLABS * K
    key_out, key_in, key_count = jax.random.split(key, 3)
    out_keys = jax.random.split(key_out, total)
    in_keys = jax.random.split(key_in, total)
    targets = jax.vmap(lambda kk: jax.random.permutation(kk, ROWS_DEV)[:RULES])(out_keys).astype(jnp.int32)
    sources = jax.vmap(lambda kk: jax.random.permutation(kk, EXT)[:RULES])(in_keys).astype(jnp.int32)
    counts = jax.random.randint(key_count, (total,), RULES // 2, RULES + 1).astype(jnp.int32)
    offset = jnp.arange(total, dtype=jnp.int32) % K
    centre = offset == K // 2
    counts = jnp.where(centre, RULES, counts)
    sources = jnp.where(centre[:, None], targets, sources)
    live = jnp.arange(RULES, dtype=jnp.int32)[None, :] < counts[:, None]
    targets = jnp.where(live, targets, ROWS_DEV)
    sources = jnp.where(live, sources, EXT)
    sources = sources.reshape(SCENES, SLABS, K, RULES)
    targets = targets.reshape(SCENES, SLABS, K, RULES)
    return jnp.stack([sources, targets], axis=2).astype(jnp.int32)


def place_ends(drawn, rng, smallest, top_value):
    place = [jax.random.randint(jax.random.fold_in(rng, axis), (), 0, length) for axis, length in enumerate(drawn.shape)]
    longest = drawn.shape.index(max(drawn.shape))
    neighbour = place[:longest] + [(place[longest] + 1) % drawn.shape[longest]] + place[longest + 1:]
    return drawn.at[tuple(place)].set(smallest).at[tuple(neighbour)].set(top_value)


def shard_levels(rng, dims, cuts, least, largest):
    def one(dim, parts):
        steps = jax.random.uniform(jax.random.fold_in(jax.random.fold_in(rng, 6), dim), (parts,), jnp.float32, least / len(cuts), largest / len(cuts))
        return jnp.repeat(jnp.exp(steps), dims[dim] // parts).reshape((-1,) + (1,) * (len(dims) - dim - 1))

    factor_of = one(*cuts[0])
    for cut in cuts[1:]:
        factor_of = factor_of * one(*cut)
    return factor_of


def noise(key, extent, spread, reach, cuts=(), kind=jnp.bfloat16):
    result = spread * jax.random.normal(key, extent, jnp.float32)
    if cuts:
        result = result * shard_levels(key, extent, cuts, -0.22, 0.18)
    return jnp.clip(result, -reach, reach).astype(kind)


def setup_inputs(seed: int = 0) -> dict:
    splits = jax.random.split(jax.random.key(seed), 8)
    return {
        "features": noise(splits[0], (SCENES, NROWS, C), 1.0, 6.0, ((0, 8), (1, 32))),
        "cotangent": noise(splits[1], (SCENES, NROWS, C), 1.0, 6.0, ((0, 8), (1, 32))),
        "weight_one": noise(splits[2], (K, C, C), (K * C // 4) ** -0.5, 0.21875),
        "weight_two": noise(splits[3], (K, C, C), (K * C // 4) ** -0.5, 0.21875),
        "rules": draw_rules(jax.random.fold_in(splits[7], 71), 0),
        "halo_send": place_ends(jax.random.randint(splits[5], (SCENES, SLABS, 2, HB), 0, BLK_DEV), jax.random.fold_in(splits[5], 1), 0, BLK_DEV - 1).astype(jnp.int32),
        "block_counts": place_ends(jax.random.randint(splits[6], (SCENES, NBLOCKS), BLOCK // 8, BLOCK + 1), jax.random.fold_in(splits[6], 1), BLOCK // 8, BLOCK).astype(jnp.int32),
    }


def mat_rows(gathered, weight):
    return jnp.einsum('krc,kcd->krd', gathered.astype(jnp.float32), weight.astype(jnp.float32), precision=lax.Precision.HIGHEST)

def mat_back(cot_rows, weight):
    return jnp.einsum('krd,kcd->krc', cot_rows.astype(jnp.float32), weight.astype(jnp.float32), precision=lax.Precision.HIGHEST)

def outer_sum(left, right):
    return jnp.einsum('krc,krd->kcd', left.astype(jnp.float32), right.astype(jnp.float32), precision=lax.Precision.HIGHEST)

def extend(table, send_rows):
    picked = jax.vmap(lambda t, idx: jnp.take(t, idx.reshape(-1), axis=0).reshape(2, HALO, C))(table, send_rows)
    zero_rim = jnp.zeros((1, HALO, C), table.dtype)
    from_left = jnp.concatenate([zero_rim, picked[:-1, 1]], axis=0)
    from_right = jnp.concatenate([picked[1:, 0], zero_rim], axis=0)
    zero_row = jnp.zeros((SLABS, 1, C), table.dtype)
    return jnp.concatenate([table, from_left, from_right, zero_row], axis=1)

def assemble(dext, send_rows):
    own = dext[:, :ROWS_DEV]
    grad_left = dext[:, ROWS_DEV:ROWS_DEV + HALO]
    grad_right = dext[:, ROWS_DEV + HALO:ROWS_DEV + 2 * HALO]
    zero_rim = jnp.zeros((1, HALO, C), jnp.float32)
    left_back = jnp.concatenate([zero_rim, grad_right[:-1]], axis=0)
    right_back = jnp.concatenate([grad_left[1:], zero_rim], axis=0)

    def add_back(rows_own, idx, first, second):
        return rows_own.at[idx[0]].add(first).at[idx[1]].add(second)
    return jax.vmap(add_back)(own, send_rows, left_back, right_back)

def reference(features, cotangent, weight_one, weight_two, rules, halo_send, block_counts):
    global_weights = jnp.stack([weight_one, weight_two])
    scene_fn = make_scene(global_weights)
    grad_rows, gw1, gw2 = lax.map(scene_fn, (features, cotangent, rules, halo_send, block_counts))
    scale = 1.0 / jnp.sqrt(jnp.float32(SCENES * SLABS * RULES))
    return (grad_rows, lax.optimization_barrier(jnp.sum(gw1, axis=0)) * scale, lax.optimization_barrier(jnp.sum(gw2, axis=0)) * scale)

def make_scene(weights):

    def scene_with(items):
        return scene_core(items, weights)
    return scene_with

def scene_core(items, weights):
    feats, cot, links, sends, counts = items
    active = (jnp.arange(BLOCK)[None, :] < counts[:, None]).astype(jnp.float32).reshape(SLABS, ROWS_DEV, 1)
    feats = feats.reshape(SLABS, ROWS_DEV, C)
    cot = cot.reshape(SLABS, ROWS_DEV, C)
    xa = feats * active.astype(jnp.bfloat16)
    ga = cot * active.astype(jnp.bfloat16)
    send_rows = (sends[:, :, :, None] * BLOCK + jnp.arange(BLOCK)[None, None, None, :]).reshape(SLABS, 2, HALO).astype(jnp.int32)
    ext_x = extend(xa, send_rows)
    weight_first = weights[0]
    weight_second = weights[1]

    def forward_slab(args):
        table, link = args
        prod = mat_rows(jnp.take(table, link[0], axis=0), weight_first)
        return jnp.zeros((ROWS_DEV + 1, C), jnp.float32).at[link[1].reshape(-1)].add(prod.reshape(-1, C))[:ROWS_DEV]
    z1 = lax.map(forward_slab, (ext_x, links))
    y1 = (jax.nn.silu(z1) * active).astype(jnp.bfloat16)
    ext_y = extend(y1, send_rows)

    def second_slab(args):
        table, cot_rows, link = args
        padded = jnp.concatenate([cot_rows, jnp.zeros((1, C), jnp.bfloat16)], axis=0)
        gga = jnp.take(padded, link[1], axis=0)
        gw = outer_sum(jnp.take(table, link[0], axis=0), gga)
        prod = mat_back(gga, weight_second)
        dext = jnp.zeros((EXT + 1, C), jnp.float32).at[link[0].reshape(-1)].add(prod.reshape(-1, C))
        return (gw, dext)
    gw2_slabs, dext_y = lax.map(second_slab, (ext_y, ga, links))
    dy1 = assemble(dext_y, send_rows)
    sig = jax.nn.sigmoid(z1)
    dz1 = (dy1 * sig * (1.0 + z1 * (1.0 - sig)) * active).astype(jnp.bfloat16)

    def first_slab(args):
        table, dz_rows, link = args
        padded = jnp.concatenate([dz_rows, jnp.zeros((1, C), jnp.bfloat16)], axis=0)
        dz_out = jnp.take(padded, link[1], axis=0)
        gw = outer_sum(jnp.take(table, link[0], axis=0), dz_out)
        prod = mat_back(dz_out, weight_first)
        dext = jnp.zeros((EXT + 1, C), jnp.float32).at[link[0].reshape(-1)].add(prod.reshape(-1, C))
        return (gw, dext)
    gw1_slabs, dext_x = lax.map(first_slab, (ext_x, dz1, links))
    grad_rows = assemble(dext_x, send_rows) * active
    return (grad_rows.reshape(NROWS, C), lax.optimization_barrier(jnp.sum(gw1_slabs, axis=0)), lax.optimization_barrier(jnp.sum(gw2_slabs, axis=0)))
```

```python
import jax
import jax.numpy as jnp
from jax import lax
from jax.sharding import PartitionSpec as P


def with_halo(block, sides, width):
    for axis, dim in sides:
        count = lax.axis_size(axis)
        forward = [(i, i + 1) for i in range(count - 1)]
        backward = [(target, source) for source, target in forward]
        low = lax.ppermute(
            lax.slice_in_dim(block, block.shape[dim] - width, None, axis=dim), axis, forward
        )
        high = lax.ppermute(lax.slice_in_dim(block, 0, width, axis=dim), axis, backward)
        block = jnp.concatenate([low, block, high], axis=dim)
    return block


def one_hot_rows(index, count):
    return (index[:, None] == jnp.arange(count, dtype=jnp.int32)[None, :]).astype(jnp.bfloat16)


def body(features, cotangent, weight_one, weight_two, rules, halo_send, block_counts):
    feats = features[0]
    cot = cotangent[0]
    links = rules[0, 0]
    sends = halo_send[0, 0]
    counts = block_counts[0]
    rows, width = feats.shape
    blocks = counts.shape[0]
    block = rows // blocks
    per_side = sends.shape[1]
    halo_rows = per_side * block
    rule_slots = links.shape[2]
    ext_rows = rows + 2 * halo_rows
    sources = links[0]
    targets = links[1]
    active = (jnp.arange(block)[None, :] < counts[:, None]).astype(jnp.float32).reshape(rows, 1)
    active_half = active.astype(jnp.bfloat16)
    xa = feats * active_half
    ga = cot * active_half
    block_pick = one_hot_rows(sends.reshape(-1), blocks)

    def pick_blocks(table):
        picked = jnp.dot(
            block_pick, table.reshape(blocks, block * width), preferred_element_type=jnp.float32
        )
        return picked.astype(jnp.bfloat16).reshape(2 * halo_rows, width)

    def add_blocks(own, back):
        pieces = jnp.concatenate([back[:halo_rows], back[3 * halo_rows :]], axis=0).reshape(
            2 * per_side, block * width
        )
        added = jnp.einsum(
            "be,bc->ec",
            block_pick.astype(jnp.float32),
            pieces,
            precision=lax.Precision.HIGHEST,
            preferred_element_type=jnp.float32,
        )
        return own + added.reshape(rows, width)

    rim_x = with_halo(pick_blocks(xa), (("space", 0),), halo_rows)
    ext_x = jnp.concatenate([xa, rim_x[:halo_rows], rim_x[3 * halo_rows :]], axis=0)
    src_pick = (sources[:, :, None] == jnp.arange(ext_rows, dtype=jnp.int32)).astype(jnp.bfloat16)
    tgt_pick = (targets[:, :, None] == jnp.arange(rows, dtype=jnp.int32)).astype(jnp.bfloat16)

    def exact(spec, a, b):
        return jnp.einsum(spec, a, b, preferred_element_type=jnp.float32).astype(jnp.bfloat16)

    gathered = exact("kre,ec->krc", src_pick, ext_x)
    placed = exact("kro,krc->koc", tgt_pick, gathered)
    z1 = jnp.einsum("koc,kcd->od", placed, weight_one, preferred_element_type=jnp.float32)
    y1 = (jax.nn.silu(z1) * active).astype(jnp.bfloat16)
    rim_y = with_halo(pick_blocks(y1), (("space", 0),), halo_rows)
    ext_y = jnp.concatenate([y1, rim_y[:halo_rows], rim_y[3 * halo_rows :]], axis=0)

    def backward(table, cot_rows, weight):
        cot_picked = exact("kro,oc->krc", tgt_pick, cot_rows)
        at_source = exact("kre,krc->kec", src_pick, cot_picked)
        dext = jnp.einsum("ked,kcd->ec", at_source, weight, preferred_element_type=jnp.float32)
        grad_kernel = jnp.einsum("ec,ked->kcd", table, at_source, preferred_element_type=jnp.float32)
        return dext, grad_kernel

    scale = 1.0 / jnp.sqrt(jnp.float32(lax.axis_size("dp") * lax.axis_size("space") * rule_slots))
    dext_y, grad_second = backward(ext_y, ga, weight_two)
    total_second = lax.psum(grad_second, ("space", "dp"))
    back_y = with_halo(dext_y[rows:], (("space", 0),), halo_rows)
    dy1 = add_blocks(dext_y[:rows], back_y)
    sig = jax.nn.sigmoid(z1)
    dz1 = (dy1 * sig * (1.0 + z1 * (1.0 - sig)) * active).astype(jnp.bfloat16)
    dext_x, grad_first = backward(ext_x, dz1, weight_one)
    back_x = with_halo(dext_x[rows:], (("space", 0),), halo_rows)
    grad_rows = add_blocks(dext_x[:rows], back_x) * active
    total_first = lax.psum(grad_first, ("space", "dp"))
    return (grad_rows[None], total_first * scale, total_second * scale)


def solution(mesh):
    in_specs = (
        P("dp", "space", None),
        P("dp", "space", None),
        P(),
        P(),
        P("dp", "space", None, None, None),
        P("dp", "space", None, None),
        P("dp", "space"),
    )
    out_specs = (P("dp", "space", None), P(), P())
    return jax.shard_map(body, mesh=mesh, in_specs=in_specs, out_specs=out_specs, check_vma=False)
```

```python
import jax
import jax.numpy as jnp
from jax import lax
from jax.sharding import PartitionSpec as P


def with_halo(block, sides, width):
    for axis, dim in sides:
        count = lax.axis_size(axis)
        forward = [(i, i + 1) for i in range(count - 1)]
        backward = [(target, source) for source, target in forward]
        low = lax.ppermute(
            lax.slice_in_dim(block, block.shape[dim] - width, None, axis=dim), axis, forward
        )
        high = lax.ppermute(lax.slice_in_dim(block, 0, width, axis=dim), axis, backward)
        block = jnp.concatenate([low, block, high], axis=dim)
    return block


def one_hot_rows(index, count):
    return (index[:, None] == jnp.arange(count, dtype=jnp.int32)[None, :]).astype(jnp.bfloat16)


def halving_orders():
    core, y0, y1 = ("dp", 0), ("dp", 1), ("dp", 2)
    z0, z1, z2, x0, x1 = ("space", 0), ("space", 1), ("space", 2), ("space", 3), ("space", 4)
    return (
        (core, y0, y1, x0, x1, z0, z1, z2),
        (core, x0, x1, z0, z1, z2, y0, y1),
        (core, z0, z1, z2, y0, y1, x0, x1),
    )


def partner_step(axis, bit):
    count = lax.axis_size(axis)
    upper = ((lax.axis_index(axis) >> bit) & 1) == 1
    return upper, [(i, i ^ (1 << bit)) for i in range(count)]


def tree_sum(total):
    orders = halving_orders()
    pieces = jnp.split(total, len(orders), axis=0)
    for step in range(len(orders[0])):
        for p, order in enumerate(orders):
            upper, pairs = partner_step(*order[step])
            half = pieces[p].shape[0] // 2
            low, high = pieces[p][:half], pieces[p][half:]
            sent = lax.ppermute(jnp.where(upper, low, high), order[step][0], pairs)
            pieces[p] = jnp.where(upper, high, low) + sent
    for step in reversed(range(len(orders[0]))):
        for p, order in enumerate(orders):
            upper, pairs = partner_step(*order[step])
            got = lax.ppermute(pieces[p], order[step][0], pairs)
            pieces[p] = jnp.where(
                upper, jnp.concatenate([got, pieces[p]]), jnp.concatenate([pieces[p], got])
            )
    return jnp.concatenate(pieces, axis=0)


def body(features, cotangent, weight_one, weight_two, rules, halo_send, block_counts):
    feats = features[0]
    cot = cotangent[0]
    links = rules[0, 0]
    sends = halo_send[0, 0]
    counts = block_counts[0]
    rows, width = feats.shape
    blocks = counts.shape[0]
    block = rows // blocks
    per_side = sends.shape[1]
    halo_rows = per_side * block
    rule_slots = links.shape[2]
    ext_rows = rows + 2 * halo_rows
    sources = links[0]
    targets = links[1]
    active = (jnp.arange(block)[None, :] < counts[:, None]).astype(jnp.float32).reshape(rows, 1)
    active_half = active.astype(jnp.bfloat16)
    xa = feats * active_half
    ga = cot * active_half
    block_pick = one_hot_rows(sends.reshape(-1), blocks)

    def pick_blocks(table):
        picked = jnp.dot(
            block_pick, table.reshape(blocks, block * width), preferred_element_type=jnp.float32
        )
        return picked.astype(jnp.bfloat16).reshape(2 * halo_rows, width)

    def add_blocks(own, back):
        pieces = jnp.concatenate([back[:halo_rows], back[3 * halo_rows :]], axis=0).reshape(
            2 * per_side, block * width
        )
        added = jnp.einsum(
            "be,bc->ec",
            block_pick.astype(jnp.float32),
            pieces,
            precision=lax.Precision.HIGHEST,
            preferred_element_type=jnp.float32,
        )
        return own + added.reshape(rows, width)

    rim_x = with_halo(pick_blocks(xa), (("space", 0),), halo_rows)
    ext_x = jnp.concatenate([xa, rim_x[:halo_rows], rim_x[3 * halo_rows :]], axis=0)
    src_pick = (sources[:, :, None] == jnp.arange(ext_rows, dtype=jnp.int32)).astype(jnp.bfloat16)
    tgt_pick = (targets[:, :, None] == jnp.arange(rows, dtype=jnp.int32)).astype(jnp.bfloat16)

    def exact(spec, a, b):
        return jnp.einsum(spec, a, b, preferred_element_type=jnp.float32).astype(jnp.bfloat16)

    gathered = exact("kre,ec->krc", src_pick, ext_x)
    placed = exact("kro,krc->koc", tgt_pick, gathered)
    z1 = jnp.einsum("koc,kcd->od", placed, weight_one, preferred_element_type=jnp.float32)
    y1 = (jax.nn.silu(z1) * active).astype(jnp.bfloat16)
    rim_y = with_halo(pick_blocks(y1), (("space", 0),), halo_rows)
    ext_y = jnp.concatenate([y1, rim_y[:halo_rows], rim_y[3 * halo_rows :]], axis=0)

    def backward(table, cot_rows, weight):
        cot_picked = exact("kro,oc->krc", tgt_pick, cot_rows)
        at_source = exact("kre,krc->kec", src_pick, cot_picked)
        dext = jnp.einsum("ked,kcd->ec", at_source, weight, preferred_element_type=jnp.float32)
        grad_kernel = jnp.einsum("ec,ked->kcd", table, at_source, preferred_element_type=jnp.float32)
        return dext, grad_kernel

    scale = 1.0 / jnp.sqrt(jnp.float32(lax.axis_size("dp") * lax.axis_size("space") * rule_slots))
    dext_y, grad_second = backward(ext_y, ga, weight_two)
    back_y = with_halo(dext_y[rows:], (("space", 0),), halo_rows)
    dy1 = add_blocks(dext_y[:rows], back_y)
    sig = jax.nn.sigmoid(z1)
    dz1 = (dy1 * sig * (1.0 + z1 * (1.0 - sig)) * active).astype(jnp.bfloat16)
    dext_x, grad_first = backward(ext_x, dz1, weight_one)
    back_x = with_halo(dext_x[rows:], (("space", 0),), halo_rows)
    grad_rows = add_blocks(dext_x[:rows], back_x) * active
    kernels = jnp.concatenate([grad_first, grad_second], axis=0).reshape(-1, width)
    total_first, total_second = jnp.split(tree_sum(kernels).reshape(-1, width, width), 2, axis=0)
    return (grad_rows[None], total_first * scale, total_second * scale)


def solution(mesh):
    in_specs = (
        P("dp", "space", None),
        P("dp", "space", None),
        P(),
        P(),
        P("dp", "space", None, None, None),
        P("dp", "space", None, None),
        P("dp", "space"),
    )
    out_specs = (P("dp", "space", None), P(), P())
    return jax.shard_map(body, mesh=mesh, in_specs=in_specs, out_specs=out_specs, check_vma=False)
```

```python
import jax
import jax.numpy as jnp
from jax import lax
from jax.sharding import PartitionSpec as P


def with_halo(block, sides, width):
    for axis, dim in sides:
        count = lax.axis_size(axis)
        forward = [(i, i + 1) for i in range(count - 1)]
        backward = [(target, source) for source, target in forward]
        low = lax.ppermute(
            lax.slice_in_dim(block, block.shape[dim] - width, None, axis=dim), axis, forward
        )
        high = lax.ppermute(lax.slice_in_dim(block, 0, width, axis=dim), axis, backward)
        block = jnp.concatenate([low, block, high], axis=dim)
    return block


def one_hot_rows(index, count):
    return (index[:, None] == jnp.arange(count, dtype=jnp.int32)[None, :]).astype(jnp.bfloat16)


def halve(values, axis, bit):
    count = lax.axis_size(axis)
    upper = ((lax.axis_index(axis) >> bit) & 1) == 1
    pairs = [(i, i ^ (1 << bit)) for i in range(count)]
    half = values.shape[0] // 2
    low, high = values[:half], values[half:]
    return jnp.where(upper, high, low) + lax.ppermute(jnp.where(upper, low, high), axis, pairs)


def double(values, axis, bit):
    count = lax.axis_size(axis)
    upper = ((lax.axis_index(axis) >> bit) & 1) == 1
    pairs = [(i, i ^ (1 << bit)) for i in range(count)]
    got = lax.ppermute(values, axis, pairs)
    return jnp.where(upper, jnp.concatenate([got, values]), jnp.concatenate([values, got]))


def tree_sum(total):
    parts = lax.axis_size("space")
    inner = [("dp", 1), ("dp", 2)]
    values = halve(total, "dp", 0)
    spread = values.reshape(parts, values.shape[0] // parts, values.shape[1])
    values = jnp.sum(lax.all_to_all(spread, "space", 0, 0, tiled=True), axis=0)
    for axis, bit in inner:
        values = halve(values, axis, bit)
    for axis, bit in reversed(inner):
        values = double(values, axis, bit)
    copies = jnp.broadcast_to(values[None], (parts,) + values.shape)
    values = lax.all_to_all(copies, "space", 0, 0, tiled=True).reshape(-1, values.shape[1])
    return double(values, "dp", 0)


def body(features, cotangent, weight_one, weight_two, rules, halo_send, block_counts):
    feats = features[0]
    cot = cotangent[0]
    links = rules[0, 0]
    sends = halo_send[0, 0]
    counts = block_counts[0]
    rows, width = feats.shape
    blocks = counts.shape[0]
    block = rows // blocks
    per_side = sends.shape[1]
    halo_rows = per_side * block
    rule_slots = links.shape[2]
    ext_rows = rows + 2 * halo_rows
    sources = links[0]
    targets = links[1]
    active = (jnp.arange(block)[None, :] < counts[:, None]).astype(jnp.float32).reshape(rows, 1)
    active_half = active.astype(jnp.bfloat16)
    xa = feats * active_half
    ga = cot * active_half
    block_pick = one_hot_rows(sends.reshape(-1), blocks)

    def pick_blocks(table):
        picked = jnp.dot(
            block_pick, table.reshape(blocks, block * width), preferred_element_type=jnp.float32
        )
        return picked.astype(jnp.bfloat16).reshape(2 * halo_rows, width)

    def add_blocks(own, back):
        pieces = jnp.concatenate([back[:halo_rows], back[3 * halo_rows :]], axis=0).reshape(
            2 * per_side, block * width
        )
        added = jnp.einsum(
            "be,bc->ec",
            block_pick.astype(jnp.float32),
            pieces,
            precision=lax.Precision.HIGHEST,
            preferred_element_type=jnp.float32,
        )
        return own + added.reshape(rows, width)

    rim_x = with_halo(pick_blocks(xa), (("space", 0),), halo_rows)
    ext_x = jnp.concatenate([xa, rim_x[:halo_rows], rim_x[3 * halo_rows :]], axis=0)
    src_pick = (sources[:, :, None] == jnp.arange(ext_rows, dtype=jnp.int32)).astype(jnp.bfloat16)
    tgt_pick = (targets[:, :, None] == jnp.arange(rows, dtype=jnp.int32)).astype(jnp.bfloat16)

    def exact(spec, a, b):
        return jnp.einsum(spec, a, b, preferred_element_type=jnp.float32).astype(jnp.bfloat16)

    gathered = exact("kre,ec->krc", src_pick, ext_x)
    placed = exact("kro,krc->koc", tgt_pick, gathered)
    z1 = jnp.einsum("koc,kcd->od", placed, weight_one, preferred_element_type=jnp.float32)
    y1 = (jax.nn.silu(z1) * active).astype(jnp.bfloat16)
    rim_y = with_halo(pick_blocks(y1), (("space", 0),), halo_rows)
    ext_y = jnp.concatenate([y1, rim_y[:halo_rows], rim_y[3 * halo_rows :]], axis=0)

    def backward(table, cot_rows, weight):
        cot_picked = exact("kro,oc->krc", tgt_pick, cot_rows)
        at_source = exact("kre,krc->kec", src_pick, cot_picked)
        dext = jnp.einsum("ked,kcd->ec", at_source, weight, preferred_element_type=jnp.float32)
        grad_kernel = jnp.einsum("ec,ked->kcd", table, at_source, preferred_element_type=jnp.float32)
        return dext, grad_kernel

    scale = 1.0 / jnp.sqrt(jnp.float32(lax.axis_size("dp") * lax.axis_size("space") * rule_slots))
    dext_y, grad_second = backward(ext_y, ga, weight_two)
    back_y = with_halo(dext_y[rows:], (("space", 0),), halo_rows)
    dy1 = add_blocks(dext_y[:rows], back_y)
    sig = jax.nn.sigmoid(z1)
    dz1 = (dy1 * sig * (1.0 + z1 * (1.0 - sig)) * active).astype(jnp.bfloat16)
    dext_x, grad_first = backward(ext_x, dz1, weight_one)
    back_x = with_halo(dext_x[rows:], (("space", 0),), halo_rows)
    grad_rows = add_blocks(dext_x[:rows], back_x) * active
    kernels = jnp.concatenate([grad_first, grad_second], axis=0).reshape(-1, width)
    total_first, total_second = jnp.split(tree_sum(kernels).reshape(-1, width, width), 2, axis=0)
    return (grad_rows[None], total_first * scale, total_second * scale)


def solution(mesh):
    in_specs = (
        P("dp", "space", None),
        P("dp", "space", None),
        P(),
        P(),
        P("dp", "space", None, None, None),
        P("dp", "space", None, None),
        P("dp", "space"),
    )
    out_specs = (P("dp", "space", None), P(), P())
    return jax.shard_map(body, mesh=mesh, in_specs=in_specs, out_specs=out_specs, check_vma=False)
```

```python
import jax
import jax.numpy as jnp
from jax import lax
from jax.sharding import PartitionSpec as P


def with_halo(block, sides, width):
    for axis, dim in sides:
        count = lax.axis_size(axis)
        forward = [(i, i + 1) for i in range(count - 1)]
        backward = [(target, source) for source, target in forward]
        low = lax.ppermute(
            lax.slice_in_dim(block, block.shape[dim] - width, None, axis=dim), axis, forward
        )
        high = lax.ppermute(lax.slice_in_dim(block, 0, width, axis=dim), axis, backward)
        block = jnp.concatenate([low, block, high], axis=dim)
    return block


def one_hot_rows(index, count):
    return (index[:, None] == jnp.arange(count, dtype=jnp.int32)[None, :]).astype(jnp.bfloat16)


def halving_orders():
    core, y0, y1 = ("dp", 0), ("dp", 1), ("dp", 2)
    z0, z1, z2, x0, x1 = ("space", 0), ("space", 1), ("space", 2), ("space", 3), ("space", 4)
    return (
        (core, y0, y1, x0, x1, z0, z1, z2),
        (core, x0, x1, z0, z1, z2, y0, y1),
        (core, z0, z1, z2, y0, y1, x0, x1),
    )


def partner_step(axis, bit):
    count = lax.axis_size(axis)
    upper = ((lax.axis_index(axis) >> bit) & 1) == 1
    return upper, [(i, i ^ (1 << bit)) for i in range(count)]


def tree_sum(total):
    orders = halving_orders()
    upper, pairs = partner_step(*orders[0][0])
    half = total.shape[0] // 2
    low, high = total[:half], total[half:]
    total = jnp.where(upper, high, low) + lax.ppermute(jnp.where(upper, low, high), "dp", pairs)
    pieces = jnp.split(total, len(orders), axis=0)
    for step in range(1, len(orders[0])):
        for p, order in enumerate(orders):
            upper, pairs = partner_step(*order[step])
            half = pieces[p].shape[0] // 2
            low, high = pieces[p][:half], pieces[p][half:]
            sent = lax.ppermute(jnp.where(upper, low, high), order[step][0], pairs)
            pieces[p] = jnp.where(upper, high, low) + sent
    pieces = [piece.astype(jnp.bfloat16) for piece in pieces]
    for step in reversed(range(1, len(orders[0]))):
        for p, order in enumerate(orders):
            upper, pairs = partner_step(*order[step])
            got = lax.ppermute(pieces[p], order[step][0], pairs)
            pieces[p] = jnp.where(
                upper, jnp.concatenate([got, pieces[p]]), jnp.concatenate([pieces[p], got])
            )
    total = jnp.concatenate(pieces, axis=0)
    upper, pairs = partner_step(*orders[0][0])
    got = lax.ppermute(total, "dp", pairs)
    total = jnp.where(upper, jnp.concatenate([got, total]), jnp.concatenate([total, got]))
    return total.astype(jnp.float32)


def body(features, cotangent, weight_one, weight_two, rules, halo_send, block_counts):
    feats = features[0]
    cot = cotangent[0]
    links = rules[0, 0]
    sends = halo_send[0, 0]
    counts = block_counts[0]
    rows, width = feats.shape
    blocks = counts.shape[0]
    block = rows // blocks
    per_side = sends.shape[1]
    halo_rows = per_side * block
    rule_slots = links.shape[2]
    ext_rows = rows + 2 * halo_rows
    sources = links[0]
    targets = links[1]
    active = (jnp.arange(block)[None, :] < counts[:, None]).astype(jnp.float32).reshape(rows, 1)
    active_half = active.astype(jnp.bfloat16)
    xa = feats * active_half
    ga = cot * active_half
    block_pick = one_hot_rows(sends.reshape(-1), blocks)

    def pick_blocks(table):
        picked = jnp.dot(
            block_pick, table.reshape(blocks, block * width), preferred_element_type=jnp.float32
        )
        return picked.astype(jnp.bfloat16).reshape(2 * halo_rows, width)

    def add_blocks(own, back):
        pieces = jnp.concatenate([back[:halo_rows], back[3 * halo_rows :]], axis=0).reshape(
            2 * per_side, block * width
        )
        added = jnp.einsum(
            "be,bc->ec",
            block_pick.astype(jnp.float32),
            pieces,
            precision=lax.Precision.HIGHEST,
            preferred_element_type=jnp.float32,
        )
        return own + added.reshape(rows, width)

    rim_x = with_halo(pick_blocks(xa), (("space", 0),), halo_rows)
    ext_x = jnp.concatenate([xa, rim_x[:halo_rows], rim_x[3 * halo_rows :]], axis=0)
    src_pick = (sources[:, :, None] == jnp.arange(ext_rows, dtype=jnp.int32)).astype(jnp.bfloat16)
    tgt_pick = (targets[:, :, None] == jnp.arange(rows, dtype=jnp.int32)).astype(jnp.bfloat16)

    def exact(spec, a, b):
        return jnp.einsum(spec, a, b, preferred_element_type=jnp.float32).astype(jnp.bfloat16)

    gathered = exact("kre,ec->krc", src_pick, ext_x)
    placed = exact("kro,krc->koc", tgt_pick, gathered)
    z1 = jnp.einsum("koc,kcd->od", placed, weight_one, preferred_element_type=jnp.float32)
    y1 = (jax.nn.silu(z1) * active).astype(jnp.bfloat16)
    rim_y = with_halo(pick_blocks(y1), (("space", 0),), halo_rows)
    ext_y = jnp.concatenate([y1, rim_y[:halo_rows], rim_y[3 * halo_rows :]], axis=0)

    def backward(table, cot_rows, weight):
        cot_picked = exact("kro,oc->krc", tgt_pick, cot_rows)
        at_source = exact("kre,krc->kec", src_pick, cot_picked)
        dext = jnp.einsum("ked,kcd->ec", at_source, weight, preferred_element_type=jnp.float32)
        grad_kernel = jnp.einsum("ec,ked->kcd", table, at_source, preferred_element_type=jnp.float32)
        return dext, grad_kernel

    scale = 1.0 / jnp.sqrt(jnp.float32(lax.axis_size("dp") * lax.axis_size("space") * rule_slots))
    dext_y, grad_second = backward(ext_y, ga, weight_two)
    back_y = with_halo(dext_y[rows:], (("space", 0),), halo_rows)
    dy1 = add_blocks(dext_y[:rows], back_y)
    sig = jax.nn.sigmoid(z1)
    dz1 = (dy1 * sig * (1.0 + z1 * (1.0 - sig)) * active).astype(jnp.bfloat16)
    dext_x, grad_first = backward(ext_x, dz1, weight_one)
    back_x = with_halo(dext_x[rows:], (("space", 0),), halo_rows)
    grad_rows = add_blocks(dext_x[:rows], back_x) * active
    kernels = jnp.concatenate([grad_first, grad_second], axis=0).reshape(-1, width)
    total_first, total_second = jnp.split(tree_sum(kernels).reshape(-1, width, width), 2, axis=0)
    return (grad_rows[None], total_first * scale, total_second * scale)


def solution(mesh):
    in_specs = (
        P("dp", "space", None),
        P("dp", "space", None),
        P(),
        P(),
        P("dp", "space", None, None, None),
        P("dp", "space", None, None),
        P("dp", "space"),
    )
    out_specs = (P("dp", "space", None), P(), P())
    return jax.shard_map(body, mesh=mesh, in_specs=in_specs, out_specs=out_specs, check_vma=False)
```

```python
import jax
import jax.numpy as jnp
from jax import lax
from jax.sharding import PartitionSpec as P


def with_halo(block, sides, width):
    for axis, dim in sides:
        count = lax.axis_size(axis)
        forward = [(i, i + 1) for i in range(count - 1)]
        backward = [(target, source) for source, target in forward]
        low = lax.ppermute(
            lax.slice_in_dim(block, block.shape[dim] - width, None, axis=dim), axis, forward
        )
        high = lax.ppermute(lax.slice_in_dim(block, 0, width, axis=dim), axis, backward)
        block = jnp.concatenate([low, block, high], axis=dim)
    return block


def one_hot_rows(index, count):
    return (index[:, None] == jnp.arange(count, dtype=jnp.int32)[None, :]).astype(jnp.bfloat16)


def halving_orders():
    core, y0, y1 = ("dp", 0), ("dp", 1), ("dp", 2)
    z0, z1, z2, x0, x1 = ("space", 0), ("space", 1), ("space", 2), ("space", 3), ("space", 4)
    return (
        (core, y0, y1, x0, x1, z0, z1, z2),
        (core, x0, x1, z0, z1, z2, y0, y1),
    )


def partner_step(axis, bit):
    count = lax.axis_size(axis)
    upper = ((lax.axis_index(axis) >> bit) & 1) == 1
    return upper, [(i, i ^ (1 << bit)) for i in range(count)]


def tree_sum(total):
    orders = halving_orders()
    upper, pairs = partner_step(*orders[0][0])
    half = total.shape[0] // 2
    low, high = total[:half], total[half:]
    total = jnp.where(upper, high, low) + lax.ppermute(jnp.where(upper, low, high), "dp", pairs)
    unit = 2 ** (len(orders[0]) - 1)
    pieces = jnp.split(total, [unit * (total.shape[0] // unit // len(orders))], axis=0)
    for step in range(1, len(orders[0])):
        for p, order in enumerate(orders):
            upper, pairs = partner_step(*order[step])
            half = pieces[p].shape[0] // 2
            low, high = pieces[p][:half], pieces[p][half:]
            sent = lax.ppermute(jnp.where(upper, low, high), order[step][0], pairs)
            pieces[p] = jnp.where(upper, high, low) + sent
    for step in reversed(range(1, len(orders[0]))):
        for p, order in enumerate(orders):
            upper, pairs = partner_step(*order[step])
            got = lax.ppermute(pieces[p], order[step][0], pairs)
            pieces[p] = jnp.where(
                upper, jnp.concatenate([got, pieces[p]]), jnp.concatenate([pieces[p], got])
            )
    total = jnp.concatenate(pieces, axis=0)
    upper, pairs = partner_step(*orders[0][0])
    got = lax.ppermute(total, "dp", pairs)
    total = jnp.where(upper, jnp.concatenate([got, total]), jnp.concatenate([total, got]))
    return total


def body(features, cotangent, weight_one, weight_two, rules, halo_send, block_counts):
    feats = features[0]
    cot = cotangent[0]
    links = rules[0, 0]
    sends = halo_send[0, 0]
    counts = block_counts[0]
    rows, width = feats.shape
    blocks = counts.shape[0]
    block = rows // blocks
    per_side = sends.shape[1]
    halo_rows = per_side * block
    rule_slots = links.shape[2]
    ext_rows = rows + 2 * halo_rows
    sources = links[0]
    targets = links[1]
    active = (jnp.arange(block)[None, :] < counts[:, None]).astype(jnp.float32).reshape(rows, 1)
    active_half = active.astype(jnp.bfloat16)
    xa = feats * active_half
    ga = cot * active_half
    block_pick = one_hot_rows(sends.reshape(-1), blocks)

    def pick_blocks(table):
        picked = jnp.dot(
            block_pick, table.reshape(blocks, block * width), preferred_element_type=jnp.float32
        )
        return picked.astype(jnp.bfloat16).reshape(2 * halo_rows, width)

    def add_blocks(own, back):
        pieces = jnp.concatenate([back[:halo_rows], back[3 * halo_rows :]], axis=0).reshape(
            2 * per_side, block * width
        )
        added = jnp.einsum(
            "be,bc->ec",
            block_pick.astype(jnp.float32),
            pieces,
            precision=lax.Precision.HIGHEST,
            preferred_element_type=jnp.float32,
        )
        return own + added.reshape(rows, width)

    rim_x = with_halo(pick_blocks(xa), (("space", 0),), halo_rows)
    ext_x = jnp.concatenate([xa, rim_x[:halo_rows], rim_x[3 * halo_rows :]], axis=0)
    src_pick = (sources[:, :, None] == jnp.arange(ext_rows, dtype=jnp.int32)).astype(jnp.bfloat16)
    tgt_pick = (targets[:, :, None] == jnp.arange(rows, dtype=jnp.int32)).astype(jnp.bfloat16)

    def exact(spec, a, b):
        return jnp.einsum(spec, a, b, preferred_element_type=jnp.float32).astype(jnp.bfloat16)

    gathered = exact("kre,ec->krc", src_pick, ext_x)
    placed = exact("kro,krc->koc", tgt_pick, gathered)
    z1 = jnp.einsum("koc,kcd->od", placed, weight_one, preferred_element_type=jnp.float32)
    y1 = (jax.nn.silu(z1) * active).astype(jnp.bfloat16)
    rim_y = with_halo(pick_blocks(y1), (("space", 0),), halo_rows)
    ext_y = jnp.concatenate([y1, rim_y[:halo_rows], rim_y[3 * halo_rows :]], axis=0)

    def backward(table, cot_rows, weight):
        cot_picked = exact("kro,oc->krc", tgt_pick, cot_rows)
        at_source = exact("kre,krc->kec", src_pick, cot_picked)
        dext = jnp.einsum("ked,kcd->ec", at_source, weight, preferred_element_type=jnp.float32)
        grad_kernel = jnp.einsum("ec,ked->kcd", table, at_source, preferred_element_type=jnp.float32)
        return dext, grad_kernel

    scale = 1.0 / jnp.sqrt(jnp.float32(lax.axis_size("dp") * lax.axis_size("space") * rule_slots))
    dext_y, grad_second = backward(ext_y, ga, weight_two)
    back_y = with_halo(dext_y[rows:], (("space", 0),), halo_rows)
    dy1 = add_blocks(dext_y[:rows], back_y)
    sig = jax.nn.sigmoid(z1)
    dz1 = (dy1 * sig * (1.0 + z1 * (1.0 - sig)) * active).astype(jnp.bfloat16)
    dext_x, grad_first = backward(ext_x, dz1, weight_one)
    back_x = with_halo(dext_x[rows:], (("space", 0),), halo_rows)
    grad_rows = add_blocks(dext_x[:rows], back_x) * active
    kernels = jnp.concatenate([grad_first, grad_second], axis=0).reshape(-1, width)
    total_first, total_second = jnp.split(tree_sum(kernels).reshape(-1, width, width), 2, axis=0)
    return (grad_rows[None], total_first * scale, total_second * scale)


def solution(mesh):
    in_specs = (
        P("dp", "space", None),
        P("dp", "space", None),
        P(),
        P(),
        P("dp", "space", None, None, None),
        P("dp", "space", None, None),
        P("dp", "space"),
    )
    out_specs = (P("dp", "space", None), P(), P())
    return jax.shard_map(body, mesh=mesh, in_specs=in_specs, out_specs=out_specs, check_vma=False)
```

```python
import jax
import jax.numpy as jnp
from jax import lax
from jax.sharding import PartitionSpec as P


def with_halo(block, sides, width):
    for axis, dim in sides:
        count = lax.axis_size(axis)
        forward = [(i, i + 1) for i in range(count - 1)]
        backward = [(target, source) for source, target in forward]
        low = lax.ppermute(
            lax.slice_in_dim(block, block.shape[dim] - width, None, axis=dim), axis, forward
        )
        high = lax.ppermute(lax.slice_in_dim(block, 0, width, axis=dim), axis, backward)
        block = jnp.concatenate([low, block, high], axis=dim)
    return block


def one_hot_rows(index, count):
    return (index[:, None] == jnp.arange(count, dtype=jnp.int32)[None, :]).astype(jnp.bfloat16)


def halving_orders():
    y0, y1 = ("dp", 1), ("dp", 2)
    z0, z1, z2, x0, x1 = ("space", 0), ("space", 1), ("space", 2), ("space", 3), ("space", 4)
    return (
        (y0, y1, x0, x1, z0, z1, z2),
        (x0, x1, z0, z1, z2, y0, y1),
        (z0, z1, z2, y0, y1, x0, x1),
    )


def partner_step(axis, bit):
    count = lax.axis_size(axis)
    upper = ((lax.axis_index(axis) >> bit) & 1) == 1
    return upper, [(i, i ^ (1 << bit)) for i in range(count)]


def tree_sum(total):
    orders = halving_orders()
    pieces = jnp.split(total, len(orders), axis=0)
    for step in range(len(orders[0])):
        for p, order in enumerate(orders):
            upper, pairs = partner_step(*order[step])
            half = pieces[p].shape[0] // 2
            low, high = pieces[p][:half], pieces[p][half:]
            sent = lax.ppermute(jnp.where(upper, low, high), order[step][0], pairs)
            pieces[p] = jnp.where(upper, high, low) + sent
    total = jnp.concatenate(pieces, axis=0)
    upper, pairs = partner_step("dp", 0)
    half = total.shape[0] // 2
    low, high = total[:half], total[half:]
    total = jnp.where(upper, high, low) + lax.ppermute(jnp.where(upper, low, high), "dp", pairs)
    got = lax.ppermute(total, "dp", pairs)
    total = jnp.where(upper, jnp.concatenate([got, total]), jnp.concatenate([total, got]))
    pieces = jnp.split(total, len(orders), axis=0)
    for step in reversed(range(len(orders[0]))):
        for p, order in enumerate(orders):
            upper, pairs = partner_step(*order[step])
            got = lax.ppermute(pieces[p], order[step][0], pairs)
            pieces[p] = jnp.where(
                upper, jnp.concatenate([got, pieces[p]]), jnp.concatenate([pieces[p], got])
            )
    return jnp.concatenate(pieces, axis=0)


def body(features, cotangent, weight_one, weight_two, rules, halo_send, block_counts):
    feats = features[0]
    cot = cotangent[0]
    links = rules[0, 0]
    sends = halo_send[0, 0]
    counts = block_counts[0]
    rows, width = feats.shape
    blocks = counts.shape[0]
    block = rows // blocks
    per_side = sends.shape[1]
    halo_rows = per_side * block
    rule_slots = links.shape[2]
    ext_rows = rows + 2 * halo_rows
    sources = links[0]
    targets = links[1]
    active = (jnp.arange(block)[None, :] < counts[:, None]).astype(jnp.float32).reshape(rows, 1)
    active_half = active.astype(jnp.bfloat16)
    xa = feats * active_half
    ga = cot * active_half
    block_pick = one_hot_rows(sends.reshape(-1), blocks)

    def pick_blocks(table):
        picked = jnp.dot(
            block_pick, table.reshape(blocks, block * width), preferred_element_type=jnp.float32
        )
        return picked.astype(jnp.bfloat16).reshape(2 * halo_rows, width)

    def add_blocks(own, back):
        pieces = jnp.concatenate([back[:halo_rows], back[3 * halo_rows :]], axis=0).reshape(
            2 * per_side, block * width
        )
        added = jnp.einsum(
            "be,bc->ec",
            block_pick.astype(jnp.float32),
            pieces,
            precision=lax.Precision.HIGHEST,
            preferred_element_type=jnp.float32,
        )
        return own + added.reshape(rows, width)

    rim_x = with_halo(pick_blocks(xa), (("space", 0),), halo_rows)
    ext_x = jnp.concatenate([xa, rim_x[:halo_rows], rim_x[3 * halo_rows :]], axis=0)
    src_pick = (sources[:, :, None] == jnp.arange(ext_rows, dtype=jnp.int32)).astype(jnp.bfloat16)
    tgt_pick = (targets[:, :, None] == jnp.arange(rows, dtype=jnp.int32)).astype(jnp.bfloat16)

    def exact(spec, a, b):
        return jnp.einsum(spec, a, b, preferred_element_type=jnp.float32).astype(jnp.bfloat16)

    gathered = exact("kre,ec->krc", src_pick, ext_x)
    placed = exact("kro,krc->koc", tgt_pick, gathered)
    z1 = jnp.einsum("koc,kcd->od", placed, weight_one, preferred_element_type=jnp.float32)
    y1 = (jax.nn.silu(z1) * active).astype(jnp.bfloat16)
    rim_y = with_halo(pick_blocks(y1), (("space", 0),), halo_rows)
    ext_y = jnp.concatenate([y1, rim_y[:halo_rows], rim_y[3 * halo_rows :]], axis=0)

    def backward(table, cot_rows, weight):
        cot_picked = exact("kro,oc->krc", tgt_pick, cot_rows)
        at_source = exact("kre,krc->kec", src_pick, cot_picked)
        dext = jnp.einsum("ked,kcd->ec", at_source, weight, preferred_element_type=jnp.float32)
        grad_kernel = jnp.einsum("ec,ked->kcd", table, at_source, preferred_element_type=jnp.float32)
        return dext, grad_kernel

    scale = 1.0 / jnp.sqrt(jnp.float32(lax.axis_size("dp") * lax.axis_size("space") * rule_slots))
    dext_y, grad_second = backward(ext_y, ga, weight_two)
    back_y = with_halo(dext_y[rows:], (("space", 0),), halo_rows)
    dy1 = add_blocks(dext_y[:rows], back_y)
    sig = jax.nn.sigmoid(z1)
    dz1 = (dy1 * sig * (1.0 + z1 * (1.0 - sig)) * active).astype(jnp.bfloat16)
    dext_x, grad_first = backward(ext_x, dz1, weight_one)
    back_x = with_halo(dext_x[rows:], (("space", 0),), halo_rows)
    grad_rows = add_blocks(dext_x[:rows], back_x) * active
    kernels = jnp.concatenate([grad_first, grad_second], axis=0).reshape(-1, width)
    total_first, total_second = jnp.split(tree_sum(kernels).reshape(-1, width, width), 2, axis=0)
    return (grad_rows[None], total_first * scale, total_second * scale)


def solution(mesh):
    in_specs = (
        P("dp", "space", None),
        P("dp", "space", None),
        P(),
        P(),
        P("dp", "space", None, None, None),
        P("dp", "space", None, None),
        P("dp", "space"),
    )
    out_specs = (P("dp", "space", None), P(), P())
    return jax.shard_map(body, mesh=mesh, in_specs=in_specs, out_specs=out_specs, check_vma=False)
```

```python
import jax
import jax.numpy as jnp
from jax import lax
from jax.sharding import PartitionSpec as P


def with_halo(block, sides, width):
    for axis, dim in sides:
        count = lax.axis_size(axis)
        forward = [(i, i + 1) for i in range(count - 1)]
        backward = [(target, source) for source, target in forward]
        low = lax.ppermute(
            lax.slice_in_dim(block, block.shape[dim] - width, None, axis=dim), axis, forward
        )
        high = lax.ppermute(lax.slice_in_dim(block, 0, width, axis=dim), axis, backward)
        block = jnp.concatenate([low, block, high], axis=dim)
    return block


def one_hot_rows(index, count):
    return (index[:, None] == jnp.arange(count, dtype=jnp.int32)[None, :]).astype(jnp.bfloat16)


def halving_orders():
    core, y0, y1 = ("dp", 0), ("dp", 1), ("dp", 2)
    z0, z1, z2, x0, x1 = ("space", 0), ("space", 1), ("space", 2), ("space", 3), ("space", 4)
    return (
        (core, y0, y1, x0, x1, z0, z1, z2),
        (core, x0, x1, z0, z1, z2, y0, y1),
    )


def partner_step(axis, bit):
    count = lax.axis_size(axis)
    upper = ((lax.axis_index(axis) >> bit) & 1) == 1
    return upper, [(i, i ^ (1 << bit)) for i in range(count)]


def tree_sum(total):
    orders = halving_orders()
    upper, pairs = partner_step(*orders[0][0])
    half = total.shape[0] // 2
    low, high = total[:half], total[half:]
    total = jnp.where(upper, high, low) + lax.ppermute(jnp.where(upper, low, high), "dp", pairs)
    unit = 2 ** (len(orders[0]) - 1)
    pieces = jnp.split(total, [unit * (total.shape[0] // unit // len(orders))], axis=0)
    for step in range(1, len(orders[0])):
        for p, order in enumerate(orders):
            upper, pairs = partner_step(*order[step])
            half = pieces[p].shape[0] // 2
            low, high = pieces[p][:half], pieces[p][half:]
            sent = lax.ppermute(jnp.where(upper, low, high), order[step][0], pairs)
            pieces[p] = jnp.where(upper, high, low) + sent
    for step in reversed(range(1, len(orders[0]))):
        for p, order in enumerate(orders):
            upper, pairs = partner_step(*order[step])
            got = lax.ppermute(pieces[p], order[step][0], pairs)
            pieces[p] = jnp.where(
                upper, jnp.concatenate([got, pieces[p]]), jnp.concatenate([pieces[p], got])
            )
    total = jnp.concatenate(pieces, axis=0)
    upper, pairs = partner_step(*orders[0][0])
    got = lax.ppermute(total, "dp", pairs)
    total = jnp.where(upper, jnp.concatenate([got, total]), jnp.concatenate([total, got]))
    return total


def body(features, cotangent, weight_one, weight_two, rules, halo_send, block_counts):
    feats = features[0]
    cot = cotangent[0]
    links = rules[0, 0]
    sends = halo_send[0, 0]
    counts = block_counts[0]
    rows, width = feats.shape
    blocks = counts.shape[0]
    block = rows // blocks
    per_side = sends.shape[1]
    halo_rows = per_side * block
    rule_slots = links.shape[2]
    ext_rows = rows + 2 * halo_rows
    sources = links[0]
    targets = links[1]
    active = (jnp.arange(block)[None, :] < counts[:, None]).astype(jnp.float32).reshape(rows, 1)
    active_half = active.astype(jnp.bfloat16)
    xa = feats * active_half
    ga = cot * active_half
    block_pick = one_hot_rows(sends.reshape(-1), blocks)

    def pick_blocks(table):
        picked = jnp.dot(
            block_pick, table.reshape(blocks, block * width), preferred_element_type=jnp.float32
        )
        return picked.astype(jnp.bfloat16).reshape(2 * halo_rows, width)

    def add_blocks(own, back):
        pieces = jnp.concatenate([back[:halo_rows], back[3 * halo_rows :]], axis=0).reshape(
            2 * per_side, block * width
        )
        added = jnp.einsum(
            "be,bc->ec",
            block_pick.astype(jnp.float32),
            pieces,
            precision=lax.Precision.HIGHEST,
            preferred_element_type=jnp.float32,
        )
        return own + added.reshape(rows, width)

    rim_x = with_halo(pick_blocks(xa), (("space", 0),), halo_rows)
    ext_x = jnp.concatenate([xa, rim_x[:halo_rows], rim_x[3 * halo_rows :]], axis=0)
    src_pick = (sources[:, :, None] == jnp.arange(ext_rows, dtype=jnp.int32)).astype(jnp.bfloat16)
    tgt_pick = (targets[:, :, None] == jnp.arange(rows, dtype=jnp.int32)).astype(jnp.bfloat16)
    src_pick, tgt_pick = lax.optimization_barrier((src_pick, tgt_pick))

    def exact(spec, a, b):
        return jnp.einsum(spec, a, b, preferred_element_type=jnp.float32).astype(jnp.bfloat16)

    gathered = exact("kre,ec->krc", src_pick, ext_x)
    placed = exact("kro,krc->koc", tgt_pick, gathered)
    z1 = jnp.einsum("koc,kcd->od", placed, weight_one, preferred_element_type=jnp.float32)
    y1 = (jax.nn.silu(z1) * active).astype(jnp.bfloat16)
    rim_y = with_halo(pick_blocks(y1), (("space", 0),), halo_rows)
    ext_y = jnp.concatenate([y1, rim_y[:halo_rows], rim_y[3 * halo_rows :]], axis=0)

    def backward(table, cot_rows, weight):
        cot_picked = exact("kro,oc->krc", tgt_pick, cot_rows)
        at_source = exact("kre,krc->kec", src_pick, cot_picked)
        dext = jnp.einsum("ked,kcd->ec", at_source, weight, preferred_element_type=jnp.float32)
        grad_kernel = jnp.einsum("ec,ked->kcd", table, at_source, preferred_element_type=jnp.float32)
        return dext, grad_kernel

    scale = 1.0 / jnp.sqrt(jnp.float32(lax.axis_size("dp") * lax.axis_size("space") * rule_slots))
    dext_y, grad_second = backward(ext_y, ga, weight_two)
    back_y = with_halo(dext_y[rows:], (("space", 0),), halo_rows)
    dy1 = add_blocks(dext_y[:rows], back_y)
    sig = jax.nn.sigmoid(z1)
    dz1 = (dy1 * sig * (1.0 + z1 * (1.0 - sig)) * active).astype(jnp.bfloat16)
    dext_x, grad_first = backward(ext_x, dz1, weight_one)
    back_x = with_halo(dext_x[rows:], (("space", 0),), halo_rows)
    grad_rows = add_blocks(dext_x[:rows], back_x) * active
    kernels = jnp.concatenate([grad_first, grad_second], axis=0).reshape(-1, width)
    total_first, total_second = jnp.split(tree_sum(kernels).reshape(-1, width, width), 2, axis=0)
    return (grad_rows[None], total_first * scale, total_second * scale)


def solution(mesh):
    in_specs = (
        P("dp", "space", None),
        P("dp", "space", None),
        P(),
        P(),
        P("dp", "space", None, None, None),
        P("dp", "space", None, None),
        P("dp", "space"),
    )
    out_specs = (P("dp", "space", None), P(), P())
    return jax.shard_map(body, mesh=mesh, in_specs=in_specs, out_specs=out_specs, check_vma=False)
```

```python
import jax
import jax.numpy as jnp
from jax import lax
from jax.sharding import PartitionSpec as P


def with_halo(block, sides, width):
    for axis, dim in sides:
        count = lax.axis_size(axis)
        forward = [(i, i + 1) for i in range(count - 1)]
        backward = [(target, source) for source, target in forward]
        low = lax.ppermute(
            lax.slice_in_dim(block, block.shape[dim] - width, None, axis=dim), axis, forward
        )
        high = lax.ppermute(lax.slice_in_dim(block, 0, width, axis=dim), axis, backward)
        block = jnp.concatenate([low, block, high], axis=dim)
    return block


def one_hot_rows(index, count):
    return (index[:, None] == jnp.arange(count, dtype=jnp.int32)[None, :]).astype(jnp.bfloat16)


def halving_orders():
    core, y0, y1 = ("dp", 0), ("dp", 1), ("dp", 2)
    z0, z1, z2, x0, x1 = ("space", 0), ("space", 1), ("space", 2), ("space", 3), ("space", 4)
    return (
        (core, y0, y1, x0, x1, z0, z1, z2),
        (core, x0, x1, z0, z1, z2, y0, y1),
    )


def partner_step(axis, bit):
    count = lax.axis_size(axis)
    upper = ((lax.axis_index(axis) >> bit) & 1) == 1
    return upper, [(i, i ^ (1 << bit)) for i in range(count)]


def core_halve(values):
    upper, pairs = partner_step("dp", 0)
    half = values.shape[0] // 2
    low, high = values[:half], values[half:]
    return jnp.where(upper, high, low) + lax.ppermute(jnp.where(upper, low, high), "dp", pairs)


def core_double(values):
    upper, pairs = partner_step("dp", 0)
    got = lax.ppermute(values, "dp", pairs)
    return jnp.where(upper, jnp.concatenate([got, values]), jnp.concatenate([values, got]))


def tree_sum(first, second):
    orders = halving_orders()
    total = jnp.concatenate([core_halve(first), second], axis=0)
    unit = 2 ** (len(orders[0]) - 1)
    pieces = jnp.split(total, [unit * (total.shape[0] // unit // len(orders))], axis=0)
    for step in range(1, len(orders[0])):
        for p, order in enumerate(orders):
            upper, pairs = partner_step(*order[step])
            half = pieces[p].shape[0] // 2
            low, high = pieces[p][:half], pieces[p][half:]
            sent = lax.ppermute(jnp.where(upper, low, high), order[step][0], pairs)
            pieces[p] = jnp.where(upper, high, low) + sent
    for step in reversed(range(1, len(orders[0]))):
        for p, order in enumerate(orders):
            upper, pairs = partner_step(*order[step])
            got = lax.ppermute(pieces[p], order[step][0], pairs)
            pieces[p] = jnp.where(
                upper, jnp.concatenate([got, pieces[p]]), jnp.concatenate([pieces[p], got])
            )
    first, second = jnp.split(jnp.concatenate(pieces, axis=0), 2, axis=0)
    return core_double(first), core_double(second)


def body(features, cotangent, weight_one, weight_two, rules, halo_send, block_counts):
    feats = features[0]
    cot = cotangent[0]
    links = rules[0, 0]
    sends = halo_send[0, 0]
    counts = block_counts[0]
    rows, width = feats.shape
    blocks = counts.shape[0]
    block = rows // blocks
    per_side = sends.shape[1]
    halo_rows = per_side * block
    rule_slots = links.shape[2]
    ext_rows = rows + 2 * halo_rows
    sources = links[0]
    targets = links[1]
    active = (jnp.arange(block)[None, :] < counts[:, None]).astype(jnp.float32).reshape(rows, 1)
    active_half = active.astype(jnp.bfloat16)
    xa = feats * active_half
    ga = cot * active_half
    block_pick = one_hot_rows(sends.reshape(-1), blocks)

    def pick_blocks(table):
        picked = jnp.dot(
            block_pick, table.reshape(blocks, block * width), preferred_element_type=jnp.float32
        )
        return picked.astype(jnp.bfloat16).reshape(2 * halo_rows, width)

    def add_blocks(own, back):
        pieces = jnp.concatenate([back[:halo_rows], back[3 * halo_rows :]], axis=0).reshape(
            2 * per_side, block * width
        )
        added = jnp.einsum(
            "be,bc->ec",
            block_pick.astype(jnp.float32),
            pieces,
            precision=lax.Precision.HIGHEST,
            preferred_element_type=jnp.float32,
        )
        return own + added.reshape(rows, width)

    rim_x = with_halo(pick_blocks(xa), (("space", 0),), halo_rows)
    ext_x = jnp.concatenate([xa, rim_x[:halo_rows], rim_x[3 * halo_rows :]], axis=0)
    src_pick = (sources[:, :, None] == jnp.arange(ext_rows, dtype=jnp.int32)).astype(jnp.bfloat16)
    tgt_pick = (targets[:, :, None] == jnp.arange(rows, dtype=jnp.int32)).astype(jnp.bfloat16)

    def exact(spec, a, b):
        return jnp.einsum(spec, a, b, preferred_element_type=jnp.float32).astype(jnp.bfloat16)

    gathered = exact("kre,ec->krc", src_pick, ext_x)
    placed = exact("kro,krc->koc", tgt_pick, gathered)
    z1 = jnp.einsum("koc,kcd->od", placed, weight_one, preferred_element_type=jnp.float32)
    y1 = (jax.nn.silu(z1) * active).astype(jnp.bfloat16)
    rim_y = with_halo(pick_blocks(y1), (("space", 0),), halo_rows)
    ext_y = jnp.concatenate([y1, rim_y[:halo_rows], rim_y[3 * halo_rows :]], axis=0)

    def backward(table, cot_rows, weight):
        cot_picked = exact("kro,oc->krc", tgt_pick, cot_rows)
        at_source = exact("kre,krc->kec", src_pick, cot_picked)
        dext = jnp.einsum("ked,kcd->ec", at_source, weight, preferred_element_type=jnp.float32)
        grad_kernel = jnp.einsum("ec,ked->kcd", table, at_source, preferred_element_type=jnp.float32)
        return dext, grad_kernel

    scale = 1.0 / jnp.sqrt(jnp.float32(lax.axis_size("dp") * lax.axis_size("space") * rule_slots))
    dext_y, grad_second = backward(ext_y, ga, weight_two)
    half_second = core_halve(grad_second.reshape(-1, width))
    back_y = with_halo(dext_y[rows:], (("space", 0),), halo_rows)
    dy1 = add_blocks(dext_y[:rows], back_y)
    sig = jax.nn.sigmoid(z1)
    dz1 = (dy1 * sig * (1.0 + z1 * (1.0 - sig)) * active).astype(jnp.bfloat16)
    dext_x, grad_first = backward(ext_x, dz1, weight_one)
    back_x = with_halo(dext_x[rows:], (("space", 0),), halo_rows)
    grad_rows = add_blocks(dext_x[:rows], back_x) * active
    total_first, total_second = tree_sum(grad_first.reshape(-1, width), half_second)
    total_first = total_first.reshape(-1, width, width)
    total_second = total_second.reshape(-1, width, width)
    return (grad_rows[None], total_first * scale, total_second * scale)


def solution(mesh):
    in_specs = (
        P("dp", "space", None),
        P("dp", "space", None),
        P(),
        P(),
        P("dp", "space", None, None, None),
        P("dp", "space", None, None),
        P("dp", "space"),
    )
    out_specs = (P("dp", "space", None), P(), P())
    return jax.shard_map(body, mesh=mesh, in_specs=in_specs, out_specs=out_specs, check_vma=False)
```

```python
import jax
import jax.numpy as jnp
from jax import lax
from jax.sharding import PartitionSpec as P


def with_halo(block, sides, width):
    for axis, dim in sides:
        count = lax.axis_size(axis)
        forward = [(i, i + 1) for i in range(count - 1)]
        backward = [(target, source) for source, target in forward]
        low = lax.ppermute(
            lax.slice_in_dim(block, block.shape[dim] - width, None, axis=dim), axis, forward
        )
        high = lax.ppermute(lax.slice_in_dim(block, 0, width, axis=dim), axis, backward)
        block = jnp.concatenate([low, block, high], axis=dim)
    return block


def one_hot_rows(index, count):
    return (index[:, None] == jnp.arange(count, dtype=jnp.int32)[None, :]).astype(jnp.bfloat16)


def halving_orders():
    core, y0, y1 = ("dp", 0), ("dp", 1), ("dp", 2)
    z0, z1, z2, x0, x1 = ("space", 0), ("space", 1), ("space", 2), ("space", 3), ("space", 4)
    return (
        (core, y0, y1, x0, x1, z0, z1, z2),
        (core, x0, x1, z0, z1, z2, y0, y1),
    )


def partner_step(axis, bit):
    count = lax.axis_size(axis)
    upper = (lax.axis_index(axis) >> bit) & 1
    return upper, [(i, i ^ (1 << bit)) for i in range(count)]


def halve_at(values, upper, axis, pairs):
    half = values.shape[0] // 2
    keep = lax.dynamic_slice_in_dim(values, upper * half, half)
    sent = lax.dynamic_slice_in_dim(values, (1 - upper) * half, half)
    return keep + lax.ppermute(sent, axis, pairs)


def double_at(values, upper, axis, pairs):
    got = lax.ppermute(values, axis, pairs)
    size = values.shape[0]
    both = jnp.concatenate([values, values])
    return lax.dynamic_update_slice_in_dim(both, got, (1 - upper) * size, 0)


def tree_sum(total):
    orders = halving_orders()
    upper, pairs = partner_step(*orders[0][0])
    total = halve_at(total, upper, "dp", pairs)
    unit = 2 ** (len(orders[0]) - 1)
    pieces = jnp.split(total, [unit * (total.shape[0] // unit // len(orders))], axis=0)
    for step in range(1, len(orders[0])):
        for p, order in enumerate(orders):
            upper, pairs = partner_step(*order[step])
            pieces[p] = halve_at(pieces[p], upper, order[step][0], pairs)
    for step in reversed(range(1, len(orders[0]))):
        for p, order in enumerate(orders):
            upper, pairs = partner_step(*order[step])
            pieces[p] = double_at(pieces[p], upper, order[step][0], pairs)
    upper, pairs = partner_step(*orders[0][0])
    return double_at(jnp.concatenate(pieces, axis=0), upper, "dp", pairs)


def body(features, cotangent, weight_one, weight_two, rules, halo_send, block_counts):
    feats = features[0]
    cot = cotangent[0]
    links = rules[0, 0]
    sends = halo_send[0, 0]
    counts = block_counts[0]
    rows, width = feats.shape
    blocks = counts.shape[0]
    block = rows // blocks
    per_side = sends.shape[1]
    halo_rows = per_side * block
    rule_slots = links.shape[2]
    ext_rows = rows + 2 * halo_rows
    sources = links[0]
    targets = links[1]
    active = (jnp.arange(block)[None, :] < counts[:, None]).astype(jnp.float32).reshape(rows, 1)
    active_half = active.astype(jnp.bfloat16)
    xa = feats * active_half
    ga = cot * active_half
    block_pick = one_hot_rows(sends.reshape(-1), blocks)

    def pick_blocks(table):
        picked = jnp.dot(
            block_pick, table.reshape(blocks, block * width), preferred_element_type=jnp.float32
        )
        return picked.astype(jnp.bfloat16).reshape(2 * halo_rows, width)

    def add_blocks(own, back):
        pieces = jnp.concatenate([back[:halo_rows], back[3 * halo_rows :]], axis=0).reshape(
            2 * per_side, block * width
        )
        added = jnp.einsum(
            "be,bc->ec",
            block_pick.astype(jnp.float32),
            pieces,
            precision=lax.Precision.HIGHEST,
            preferred_element_type=jnp.float32,
        )
        return own + added.reshape(rows, width)

    rim_x = with_halo(pick_blocks(xa), (("space", 0),), halo_rows)
    ext_x = jnp.concatenate([xa, rim_x[:halo_rows], rim_x[3 * halo_rows :]], axis=0)
    src_pick = (sources[:, :, None] == jnp.arange(ext_rows, dtype=jnp.int32)).astype(jnp.bfloat16)
    tgt_pick = (targets[:, :, None] == jnp.arange(rows, dtype=jnp.int32)).astype(jnp.bfloat16)

    def exact(spec, a, b):
        return jnp.einsum(spec, a, b, preferred_element_type=jnp.float32).astype(jnp.bfloat16)

    gathered = exact("kre,ec->krc", src_pick, ext_x)
    placed = exact("kro,krc->koc", tgt_pick, gathered)
    z1 = jnp.einsum("koc,kcd->od", placed, weight_one, preferred_element_type=jnp.float32)
    y1 = (jax.nn.silu(z1) * active).astype(jnp.bfloat16)
    rim_y = with_halo(pick_blocks(y1), (("space", 0),), halo_rows)
    ext_y = jnp.concatenate([y1, rim_y[:halo_rows], rim_y[3 * halo_rows :]], axis=0)

    def backward(table, cot_rows, weight):
        cot_picked = exact("kro,oc->krc", tgt_pick, cot_rows)
        at_source = exact("kre,krc->kec", src_pick, cot_picked)
        dext = jnp.einsum("ked,kcd->ec", at_source, weight, preferred_element_type=jnp.float32)
        grad_kernel = jnp.einsum("ec,ked->kcd", table, at_source, preferred_element_type=jnp.float32)
        return dext, grad_kernel

    scale = 1.0 / jnp.sqrt(jnp.float32(lax.axis_size("dp") * lax.axis_size("space") * rule_slots))
    dext_y, grad_second = backward(ext_y, ga, weight_two)
    back_y = with_halo(dext_y[rows:], (("space", 0),), halo_rows)
    dy1 = add_blocks(dext_y[:rows], back_y)
    sig = jax.nn.sigmoid(z1)
    dz1 = (dy1 * sig * (1.0 + z1 * (1.0 - sig)) * active).astype(jnp.bfloat16)
    dext_x, grad_first = backward(ext_x, dz1, weight_one)
    back_x = with_halo(dext_x[rows:], (("space", 0),), halo_rows)
    grad_rows = add_blocks(dext_x[:rows], back_x) * active
    kernels = jnp.concatenate([grad_first, grad_second], axis=0).reshape(-1, width)
    total_first, total_second = jnp.split(tree_sum(kernels).reshape(-1, width, width), 2, axis=0)
    return (grad_rows[None], total_first * scale, total_second * scale)


def solution(mesh):
    in_specs = (
        P("dp", "space", None),
        P("dp", "space", None),
        P(),
        P(),
        P("dp", "space", None, None, None),
        P("dp", "space", None, None),
        P("dp", "space"),
    )
    out_specs = (P("dp", "space", None), P(), P())
    return jax.shard_map(body, mesh=mesh, in_specs=in_specs, out_specs=out_specs, check_vma=False)
```

```python
import jax
import jax.numpy as jnp
from jax import lax
from jax.sharding import PartitionSpec as P


def with_halo(block, sides, width):
    for axis, dim in sides:
        count = lax.axis_size(axis)
        forward = [(i, i + 1) for i in range(count - 1)]
        backward = [(target, source) for source, target in forward]
        low = lax.ppermute(
            lax.slice_in_dim(block, block.shape[dim] - width, None, axis=dim), axis, forward
        )
        high = lax.ppermute(lax.slice_in_dim(block, 0, width, axis=dim), axis, backward)
        block = jnp.concatenate([low, block, high], axis=dim)
    return block


def one_hot_rows(index, count):
    return (index[:, None] == jnp.arange(count, dtype=jnp.int32)[None, :]).astype(jnp.bfloat16)


def halving_orders():
    core, y0, y1 = ("dp", 0), ("dp", 1), ("dp", 2)
    z0, z1, z2, x0, x1 = ("space", 0), ("space", 1), ("space", 2), ("space", 3), ("space", 4)
    return (
        (core, y0, y1, x0, x1, z0, z1, z2),
        (core, x0, x1, z0, z1, z2, y0, y1),
    )


def partner_step(axis, bit):
    count = lax.axis_size(axis)
    upper = ((lax.axis_index(axis) >> bit) & 1) == 1
    return upper, [(i, i ^ (1 << bit)) for i in range(count)]


def tree_sum(total):
    orders = halving_orders()
    upper, pairs = partner_step(*orders[0][0])
    half = total.shape[0] // 2
    low, high = total[:half], total[half:]
    total = jnp.where(upper, high, low) + lax.ppermute(jnp.where(upper, low, high), "dp", pairs)
    unit = 2 ** (len(orders[0]) - 1)
    pieces = jnp.split(total, [unit * (total.shape[0] // unit // len(orders))], axis=0)
    for step in range(1, len(orders[0])):
        for p, order in enumerate(orders):
            upper, pairs = partner_step(*order[step])
            half = pieces[p].shape[0] // 2
            low, high = pieces[p][:half], pieces[p][half:]
            sent = lax.ppermute(jnp.where(upper, low, high), order[step][0], pairs)
            pieces[p] = jnp.where(upper, high, low) + sent
    pieces = [piece.astype(jnp.bfloat16) for piece in pieces]
    for step in reversed(range(1, len(orders[0]))):
        for p, order in enumerate(orders):
            upper, pairs = partner_step(*order[step])
            got = lax.ppermute(pieces[p], order[step][0], pairs)
            pieces[p] = jnp.where(
                upper, jnp.concatenate([got, pieces[p]]), jnp.concatenate([pieces[p], got])
            )
    total = jnp.concatenate(pieces, axis=0)
    upper, pairs = partner_step(*orders[0][0])
    got = lax.ppermute(total, "dp", pairs)
    total = jnp.where(upper, jnp.concatenate([got, total]), jnp.concatenate([total, got]))
    return total.astype(jnp.float32)


def body(features, cotangent, weight_one, weight_two, rules, halo_send, block_counts):
    feats = features[0]
    cot = cotangent[0]
    links = rules[0, 0]
    sends = halo_send[0, 0]
    counts = block_counts[0]
    rows, width = feats.shape
    blocks = counts.shape[0]
    block = rows // blocks
    per_side = sends.shape[1]
    halo_rows = per_side * block
    rule_slots = links.shape[2]
    ext_rows = rows + 2 * halo_rows
    sources = links[0]
    targets = links[1]
    active = (jnp.arange(block)[None, :] < counts[:, None]).astype(jnp.float32).reshape(rows, 1)
    active_half = active.astype(jnp.bfloat16)
    xa = feats * active_half
    ga = cot * active_half
    block_pick = one_hot_rows(sends.reshape(-1), blocks)

    def pick_blocks(table):
        picked = jnp.dot(
            block_pick, table.reshape(blocks, block * width), preferred_element_type=jnp.float32
        )
        return picked.astype(jnp.bfloat16).reshape(2 * halo_rows, width)

    def add_blocks(own, back):
        pieces = jnp.concatenate([back[:halo_rows], back[3 * halo_rows :]], axis=0).reshape(
            2 * per_side, block * width
        )
        added = jnp.einsum(
            "be,bc->ec",
            block_pick.astype(jnp.float32),
            pieces,
            precision=lax.Precision.HIGHEST,
            preferred_element_type=jnp.float32,
        )
        return own + added.reshape(rows, width)

    rim_x = with_halo(pick_blocks(xa), (("space", 0),), halo_rows)
    ext_x = jnp.concatenate([xa, rim_x[:halo_rows], rim_x[3 * halo_rows :]], axis=0)
    src_pick = (sources[:, :, None] == jnp.arange(ext_rows, dtype=jnp.int32)).astype(jnp.bfloat16)
    tgt_pick = (targets[:, :, None] == jnp.arange(rows, dtype=jnp.int32)).astype(jnp.bfloat16)

    def exact(spec, a, b):
        return jnp.einsum(spec, a, b, preferred_element_type=jnp.float32).astype(jnp.bfloat16)

    gathered = exact("kre,ec->krc", src_pick, ext_x)
    placed = exact("kro,krc->koc", tgt_pick, gathered)
    z1 = jnp.einsum("koc,kcd->od", placed, weight_one, preferred_element_type=jnp.float32)
    y1 = (jax.nn.silu(z1) * active).astype(jnp.bfloat16)
    rim_y = with_halo(pick_blocks(y1), (("space", 0),), halo_rows)
    ext_y = jnp.concatenate([y1, rim_y[:halo_rows], rim_y[3 * halo_rows :]], axis=0)

    def backward(table, cot_rows, weight):
        cot_picked = exact("kro,oc->krc", tgt_pick, cot_rows)
        at_source = exact("kre,krc->kec", src_pick, cot_picked)
        dext = jnp.einsum("ked,kcd->ec", at_source, weight, preferred_element_type=jnp.float32)
        grad_kernel = jnp.einsum("ec,ked->kcd", table, at_source, preferred_element_type=jnp.float32)
        return dext, grad_kernel

    scale = 1.0 / jnp.sqrt(jnp.float32(lax.axis_size("dp") * lax.axis_size("space") * rule_slots))
    dext_y, grad_second = backward(ext_y, ga, weight_two)
    back_y = with_halo(dext_y[rows:], (("space", 0),), halo_rows)
    dy1 = add_blocks(dext_y[:rows], back_y)
    sig = jax.nn.sigmoid(z1)
    dz1 = (dy1 * sig * (1.0 + z1 * (1.0 - sig)) * active).astype(jnp.bfloat16)
    dext_x, grad_first = backward(ext_x, dz1, weight_one)
    back_x = with_halo(dext_x[rows:], (("space", 0),), halo_rows)
    grad_rows = add_blocks(dext_x[:rows], back_x) * active
    kernels = jnp.concatenate([grad_first, grad_second], axis=0).reshape(-1, width)
    total_first, total_second = jnp.split(tree_sum(kernels).reshape(-1, width, width), 2, axis=0)
    return (grad_rows[None], total_first * scale, total_second * scale)


def solution(mesh):
    in_specs = (
        P("dp", "space", None),
        P("dp", "space", None),
        P(),
        P(),
        P("dp", "space", None, None, None),
        P("dp", "space", None, None),
        P("dp", "space"),
    )
    out_specs = (P("dp", "space", None), P(), P())
    return jax.shard_map(body, mesh=mesh, in_specs=in_specs, out_specs=out_specs, check_vma=False)
```
